128 devices in a mesh: cfg: 2 (over core), row: 4 (over z), col: 16 (over y, x).
Axes of the slice: x: 4, y: 4, z: 4, core: 2. Of those that a mesh axis runs over, the one named last changes fastest.
Arguments:
- img_tokens: bfloat16 [2, 16, 1024, 3072], P('cfg', 'col', None, 'row'), may hold values from -6 to 6
- txt_tokens: bfloat16 [2, 16, 512, 3072], P('cfg', 'col', None, 'row'), may hold values from -6 to 6
- img_mod: bfloat16 [2, 16, 2, 3072], P('cfg', 'col', None, 'row'), may hold values from -3 to 3
- txt_mod: bfloat16 [2, 16, 2, 3072], P('cfg', 'col', None, 'row'), may hold values from -3 to 3
- img_gate: bfloat16 [2, 16, 3072], P('cfg', 'col', 'row'), may hold values from -16 to 16
- txt_len: int32 [2, 16], P('cfg', 'col'), may hold values from 128 to 512, as said below
- img_qkv_weight: bfloat16 [3072, 3, 3072], P('col', None, 'row'), may hold values from -0.109375 to 0.109375
- txt_kv_weight: bfloat16 [3072, 2, 3072], P('col', None, 'row'), may hold values from -0.109375 to 0.109375
- out_weight: bfloat16 [3072, 3072], P('row', 'col'), may hold values from -0.109375 to 0.109375
- final_weight: bfloat16 [3072, 64], P('row'), may hold values from -0.109375 to 0.109375
- latent: float32 [16, 1024, 64], P('col', ('cfg', 'row')), may hold values from -6 to 6
- sigmas: float32 [5], replicated, may hold values from 0 to 2, as said below
- step_index: int32 [1], replicated, may hold values from 0 to 3
- guidance: float32 [1], replicated, may hold values from 1.5 to 5
Outputs:
- img_out: bfloat16 [2, 16, 1024, 3072], P('cfg', 'col', None, 'row')
- latent_next: float32 [16, 1024, 64], P('col', ('cfg', 'row'))
The draws below stay inside these ranges and needn't reach their ends.
Inputs may be any that keep to these rules, and one draw needn't show every extreme that they name: `txt_len`: in each half some prompt has all 512 text slots live and some other prompt exactly 128. `sigmas`: falls strictly along the table.
All inputs are finite; a program needn't handle non-finite values.
Results may differ from the reference program's by a relative error of at most 0.015.
Values may be sent and summed in bfloat16 or wider, within the bound.
No kernel may reach another device: no remote copies, remote signals or barrier semaphores. Data moves between devices by JAX's collectives and lax.ppermute only.
A program may use at most 128 MiB of HBM per device.

```python
import math
import jax
import jax.numpy as jnp
from jax import lax

D = 3072
HEADS = 24
HD = 128
C = 64
IMG = 1024
TXT = 512
STEPS = 4
P_SIZE = 16
N_ROW = 4


def draw_txt_len(key, part):
    lengths = jax.random.randint(key, (2, P_SIZE), TXT // 4, TXT + 1)
    top_slot = jax.random.randint(jax.random.fold_in(key, 1), (2, 1), 0, P_SIZE)
    step_over = jax.random.randint(jax.random.fold_in(key, 2), (2, 1), 1, P_SIZE)
    low_slot = (top_slot + step_over) % P_SIZE
    slots = jnp.arange(P_SIZE, dtype=jnp.int32)[None, :]
    lengths = jnp.where(slots == top_slot, TXT, lengths)
    lengths = jnp.where(slots == low_slot, TXT // 4, lengths)
    return lengths.astype(jnp.int32)


def draw_sigmas(key, part):
    jitter = 0.5 * jax.random.uniform(key, (STEPS + 1,), jnp.float32)
    levels = jnp.arange(STEPS + 1, dtype=jnp.float32)
    return ((STEPS - levels + jitter) / STEPS).astype(jnp.float32)


def block_levels(key, shape, shards, least, high):
    level = 1.0
    for position, parts in shards:
        steps = jax.random.uniform(jax.random.fold_in(jax.random.fold_in(key, 6), position), (parts,), jnp.float32, least / len(shards), high / len(shards))
        level = level * jnp.repeat(jnp.exp(steps), shape[position] // parts).reshape((-1,) + (1,) * (len(shape) - 1 - position))
    return level


def bell_draw(key, shape, width, reach, pieces=(), kind=jnp.bfloat16):
    level = block_levels(key, shape, pieces, -0.22, 0.18) if pieces else 1.0
    drawn = jax.random.normal(key, shape, jnp.float32) * width * level
    return jnp.minimum(jnp.maximum(drawn, -reach), reach).astype(kind)


def setup_inputs(seed: int = 0) -> dict:
    key_of = jax.random.split(jax.random.key(seed), 15)
    img_tokens = bell_draw(key_of[0], (2, P_SIZE, IMG, D), 1.0, 6.0, ((0, 2), (1, 16), (3, 4)))
    txt_tokens = bell_draw(key_of[1], (2, P_SIZE, TXT, D), 1.0, 6.0, ((0, 2), (1, 16), (3, 4)))
    img_mod = bell_draw(key_of[2], (2, P_SIZE, 2, D), 0.5, 3.0, ((0, 2), (1, 16), (3, 4)))
    txt_mod = bell_draw(key_of[3], (2, P_SIZE, 2, D), 0.5, 3.0, ((0, 2), (1, 16), (3, 4)))
    img_gate = bell_draw(key_of[4], (2, P_SIZE, D), 4.0, 16.0, ((0, 2), (1, 16), (2, 4)))
    txt_len = draw_txt_len(jax.random.fold_in(key_of[14], 71), 0)
    img_qkv_weight = bell_draw(key_of[6], (D, 3, D), D ** -0.5, 0.109375, ((0, 16), (2, 4)))
    txt_kv_weight = bell_draw(key_of[7], (D, 2, D), D ** -0.5, 0.109375, ((0, 16), (2, 4)))
    out_weight = bell_draw(key_of[8], (D, D), D ** -0.5, 0.109375, ((0, 4), (1, 16)))
    final_weight = bell_draw(key_of[9], (D, C), D ** -0.5, 0.109375, ((0, 4),))
    latent = bell_draw(key_of[10], (P_SIZE, IMG, C), 1.0, 6.0, ((0, 16), (1, 8)), jnp.float32)
    sigmas = draw_sigmas(jax.random.fold_in(key_of[14], 71), 0)
    step_index = jax.random.randint(key_of[12], (1,), 0, STEPS).astype(jnp.int32)
    guidance = jnp.clip(jax.random.uniform(key_of[13], (1,), jnp.float32, 1.5, 5.0), 1.5, 5.0)
    return {"img_tokens": img_tokens, "txt_tokens": txt_tokens, "img_mod": img_mod, "txt_mod": txt_mod, "img_gate": img_gate, "txt_len": txt_len, "img_qkv_weight": img_qkv_weight, "txt_kv_weight": txt_kv_weight, "out_weight": out_weight, "final_weight": final_weight, "latent": latent, "sigmas": sigmas, "step_index": step_index, "guidance": guidance}


def modulate(tokens, shift_scale):
    values = tokens.astype(jnp.float32)
    centre = values - lax.optimization_barrier(jnp.mean(values, -1, keepdims=True))
    spread = lax.optimization_barrier(jnp.mean(centre * centre, -1, keepdims=True))
    normed = centre * lax.rsqrt(spread + 1e-06)
    scaled = normed * (1.0 + shift_scale[..., 1:2, :].astype(jnp.float32))
    return (scaled + shift_scale[..., 0:1, :].astype(jnp.float32)).astype(jnp.bfloat16)

def rms_norm(values):
    return values * lax.rsqrt(lax.optimization_barrier(jnp.mean(values * values, -1, keepdims=True)) + 1e-06)

def reference(img_tokens, txt_tokens, img_mod, txt_mod, img_gate, txt_len, img_qkv_weight, txt_kv_weight, out_weight, final_weight, latent, sigmas, step_index, guidance):

    def one_prompt(items):
        tokens, texts, img_shift, txt_shift, gating, length = items
        img_ready = modulate(tokens, img_shift)
        txt_ready = modulate(texts, txt_shift)
        img_proj = jnp.dot(img_ready, img_qkv_weight.reshape(D, 3 * D), preferred_element_type=jnp.float32)
        img_proj = img_proj.reshape(IMG, 3, HEADS, HD)
        txt_proj = jnp.dot(txt_ready, txt_kv_weight.reshape(D, 2 * D), preferred_element_type=jnp.float32)
        txt_proj = txt_proj.reshape(TXT, 2, HEADS, HD)
        queries = rms_norm(img_proj[:, 0]).astype(jnp.bfloat16)
        key_rows = jnp.concatenate([rms_norm(txt_proj[:, 0]), rms_norm(img_proj[:, 1])], 0).astype(jnp.bfloat16)
        value_rows = jnp.concatenate([txt_proj[:, 1], img_proj[:, 2]], 0).astype(jnp.bfloat16)
        scores = jnp.einsum('qhe,khe->hqk', queries.astype(jnp.float32), key_rows.astype(jnp.float32)) / math.sqrt(HD)
        positions = jnp.arange(TXT + IMG, dtype=jnp.int32)
        usable = (positions < length) | (positions >= TXT)
        weights = jnp.where(usable, jnp.exp(scores), 0.0)
        chances = (weights / lax.optimization_barrier(jnp.sum(weights, -1, keepdims=True))).astype(jnp.bfloat16)
        attended = jnp.einsum('hqk,khe->qhe', chances.astype(jnp.float32), value_rows.astype(jnp.float32))
        attended = attended.reshape(IMG, D).astype(jnp.bfloat16)
        group_width = D // N_ROW
        terms = jnp.einsum('inr,nrd->nid', attended.reshape(IMG, N_ROW, group_width).astype(jnp.float32), out_weight.reshape(N_ROW, group_width, D).astype(jnp.float32))
        projected = lax.optimization_barrier(jnp.sum(terms.astype(jnp.bfloat16).astype(jnp.float32), 0))
        img_out = (tokens.astype(jnp.float32) + gating[None, :].astype(jnp.float32) * projected).astype(jnp.bfloat16)
        velocity = jnp.dot(img_out, final_weight, preferred_element_type=jnp.float32)
        return (img_out, velocity)
    outputs = []
    speeds = []
    for half in range(2):
        img_out, velocity = lax.map(one_prompt, (img_tokens[half], txt_tokens[half], img_mod[half], txt_mod[half], img_gate[half], txt_len[half]))
        outputs.append(img_out)
        speeds.append(velocity)
    strength = guidance[0]
    guided = speeds[0] * (1.0 - strength) + speeds[1] * strength
    position_now = step_index[0]
    step_size = sigmas[position_now + 1] - sigmas[position_now]
    return (jnp.stack(outputs), latent + step_size * guided)
```

```python
import math

import jax
import jax.numpy as jnp
from jax import lax
from jax.sharding import PartitionSpec as P

HD = 128


def rms_norm(values):
    return values * lax.rsqrt(jnp.mean(values * values, -1, keepdims=True) + 1e-06)


def shift_pairs(size, step):
    return [(i, (i + step) % size) for i in range(size)]


def ring_gather(piece, axis_name, size):
    assert size == 4
    from_prev = lax.ppermute(piece, axis_name, shift_pairs(size, 1))
    from_next = lax.ppermute(piece, axis_name, shift_pairs(size, -1))
    cut = piece.shape[0] // 2
    far_top = lax.ppermute(from_prev[:cut], axis_name, shift_pairs(size, 1))
    far_bottom = lax.ppermute(from_next[cut:], axis_name, shift_pairs(size, -1))
    far = jnp.concatenate([far_top, far_bottom], 0)
    return [piece, from_next, far, from_prev]


def modulate_blocks(blocks, mods, width):
    values = [b.astype(jnp.float32) for b in blocks]
    mean = sum(jnp.sum(v, -1, keepdims=True) for v in values) / width
    centred = [v - mean for v in values]
    spread = sum(jnp.sum(c * c, -1, keepdims=True) for c in centred) / width
    scale = lax.rsqrt(spread + 1e-06)
    out = []
    for c, m in zip(centred, mods):
        m = m.astype(jnp.float32)
        out.append(((c * scale) * (1.0 + m[1:2]) + m[0:1]).astype(jnp.bfloat16))
    return jnp.concatenate(out, -1)


def add_rows(piece, ready):
    return jnp.dot(ready, piece.reshape(piece.shape[0], -1), preferred_element_type=jnp.float32)


def shards(
    img_tokens,
    txt_tokens,
    img_mod,
    txt_mod,
    img_gate,
    txt_len,
    img_qkv_weight,
    txt_kv_weight,
    out_weight,
    final_weight,
    latent,
    sigmas,
    step_index,
    guidance,
):
    n_row = 4
    images = img_tokens.shape[2]
    text_slots = txt_tokens.shape[2]
    local_width = img_qkv_weight.shape[2]
    width = local_width * n_row
    heads_here = local_width // HD
    me_row = lax.axis_index("row")
    core = lax.axis_index("cfg")

    bundle = jnp.concatenate(
        [img_tokens[0, 0], img_mod[0, 0], txt_tokens[0, 0], txt_mod[0, 0]], 0
    )
    by_offset = jnp.stack(ring_gather(bundle, "row", n_row))
    blocks = [
        lax.dynamic_index_in_dim(by_offset, (k - me_row) % n_row, 0, keepdims=False)
        for k in range(n_row)
    ]
    txt_base = images + 2
    img_ready = modulate_blocks(
        [b[:images] for b in blocks], [b[images : images + 2] for b in blocks], width
    )
    txt_ready = modulate_blocks(
        [b[txt_base : txt_base + text_slots] for b in blocks],
        [b[txt_base + text_slots : txt_base + text_slots + 2] for b in blocks],
        width,
    )

    img_proj = add_rows(lax.all_gather(img_qkv_weight, "col", axis=0, tiled=True), img_ready)
    txt_proj = add_rows(lax.all_gather(txt_kv_weight, "col", axis=0, tiled=True), txt_ready)
    img_proj = img_proj.reshape(images, 3, heads_here, HD)
    txt_proj = txt_proj.reshape(text_slots, 2, heads_here, HD)
    queries = rms_norm(img_proj[:, 0]).astype(jnp.bfloat16)
    key_rows = jnp.concatenate(
        [rms_norm(txt_proj[:, 0]), rms_norm(img_proj[:, 1])], 0
    ).astype(jnp.bfloat16)
    value_rows = jnp.concatenate([txt_proj[:, 1], img_proj[:, 2]], 0).astype(jnp.bfloat16)
    positions = jnp.arange(text_slots + images, dtype=jnp.int32)
    scores = jnp.einsum(
        "qhe,khe->hqk", queries, key_rows, preferred_element_type=jnp.float32
    ) / math.sqrt(HD)
    usable = (positions < txt_len[0, 0]) | (positions >= text_slots)
    weights = jnp.where(usable, jnp.exp(scores), 0.0)
    chances = (weights / jnp.sum(weights, -1, keepdims=True)).astype(jnp.bfloat16)
    mixed = jnp.einsum("hqk,khe->qhe", chances, value_rows, preferred_element_type=jnp.float32)
    outputs = mixed.reshape(images, local_width).astype(jnp.bfloat16)
    head_terms = jnp.dot(
        outputs,
        lax.all_gather(out_weight, "col", axis=1, tiled=True),
        preferred_element_type=jnp.float32,
    ).astype(jnp.bfloat16)
    term_blocks = head_terms.reshape(images, n_row, local_width)
    projected = lax.dynamic_index_in_dim(term_blocks, me_row, 1, keepdims=False).astype(jnp.float32)
    for step in range(1, n_row):
        outgoing = lax.dynamic_index_in_dim(term_blocks, (me_row + step) % n_row, 1, keepdims=False)
        projected = projected + lax.ppermute(outgoing, "row", shift_pairs(n_row, step)).astype(
            jnp.float32
        )
    gating = img_gate[0].astype(jnp.float32)
    img_out = (img_tokens[0, 0].astype(jnp.float32) + gating * projected).astype(jnp.bfloat16)
    velocity = jnp.dot(img_out, final_weight, preferred_element_type=jnp.float32)
    strength = guidance[0]
    share = jnp.where(core == 1, strength, 1.0 - strength)
    weighted = velocity * share
    n_pair = 2 * n_row
    me_pair = core * n_row + me_row
    rows_each = weighted.shape[0] // n_pair
    velocity_blocks = weighted.reshape(n_pair, rows_each, weighted.shape[1])
    guided = lax.dynamic_index_in_dim(velocity_blocks, me_pair, 0, keepdims=False)
    for step in range(1, n_pair):
        outgoing = lax.dynamic_index_in_dim(velocity_blocks, (me_pair + step) % n_pair, 0, keepdims=False)
        guided = guided + lax.ppermute(outgoing, ("cfg", "row"), shift_pairs(n_pair, step))
    position_now = step_index[0]
    step_size = sigmas[position_now + 1] - sigmas[position_now]
    return (img_out[None, None], latent + step_size * guided[None])


def solution(mesh):
    return jax.shard_map(
        shards,
        mesh=mesh,
        in_specs=(
            P("cfg", "col", None, "row"),
            P("cfg", "col", None, "row"),
            P("cfg", "col", None, "row"),
            P("cfg", "col", None, "row"),
            P("cfg", "col", "row"),
            P("cfg", "col"),
            P("col", None, "row"),
            P("col", None, "row"),
            P("row", "col"),
            P("row", None),
            P("col", ("cfg", "row"), None),
            P(),
            P(),
            P(),
        ),
        out_specs=(P("cfg", "col", None, "row"), P("col", ("cfg", "row"), None)),
        check_vma=False,
    )
```

```python
import math

import jax
import jax.numpy as jnp
from jax import lax
from jax.sharding import PartitionSpec as P

HD = 128


def rms_norm(values):
    return values * lax.rsqrt(jnp.mean(values * values, -1, keepdims=True) + 1e-06)


def shift_pairs(size, step):
    return [(i, (i + step) % size) for i in range(size)]


def ring_gather(piece, axis_name, size):
    assert size == 4
    from_prev = lax.ppermute(piece, axis_name, shift_pairs(size, 1))
    from_next = lax.ppermute(piece, axis_name, shift_pairs(size, -1))
    cut = piece.shape[0] // 2
    far_top = lax.ppermute(from_prev[:cut], axis_name, shift_pairs(size, 1))
    far_bottom = lax.ppermute(from_next[cut:], axis_name, shift_pairs(size, -1))
    far = jnp.concatenate([far_top, far_bottom], 0)
    return [piece, from_next, far, from_prev]


def modulate_blocks(blocks, mods, width):
    values = [b.astype(jnp.float32) for b in blocks]
    mean = sum(jnp.sum(v, -1, keepdims=True) for v in values) / width
    centred = [v - mean for v in values]
    spread = sum(jnp.sum(c * c, -1, keepdims=True) for c in centred) / width
    scale = lax.rsqrt(spread + 1e-06)
    out = []
    for c, m in zip(centred, mods):
        m = m.astype(jnp.float32)
        out.append(((c * scale) * (1.0 + m[1:2]) + m[0:1]).astype(jnp.bfloat16))
    return jnp.concatenate(out, -1)


def add_rows(piece, ready):
    return jnp.dot(ready, piece.reshape(piece.shape[0], -1), preferred_element_type=jnp.float32)


def shards(
    img_tokens,
    txt_tokens,
    img_mod,
    txt_mod,
    img_gate,
    txt_len,
    img_qkv_weight,
    txt_kv_weight,
    out_weight,
    final_weight,
    latent,
    sigmas,
    step_index,
    guidance,
):
    n_row = 4
    images = img_tokens.shape[2]
    text_slots = txt_tokens.shape[2]
    local_width = img_qkv_weight.shape[2]
    width = local_width * n_row
    heads_here = local_width // HD
    me_row = lax.axis_index("row")
    core = lax.axis_index("cfg")

    pad_rows = (-(images + text_slots + 4)) % 32
    bundle = jnp.concatenate(
        [
            img_tokens[0, 0],
            txt_tokens[0, 0],
            img_mod[0, 0],
            txt_mod[0, 0],
            jnp.zeros((pad_rows, local_width), img_tokens.dtype),
        ],
        0,
    )
    by_offset = jnp.stack(ring_gather(bundle, "row", n_row))
    blocks = [
        lax.dynamic_index_in_dim(by_offset, (k - me_row) % n_row, 0, keepdims=False)
        for k in range(n_row)
    ]
    mod_base = images + text_slots
    img_ready = modulate_blocks(
        [b[:images] for b in blocks], [b[mod_base : mod_base + 2] for b in blocks], width
    )
    txt_ready = modulate_blocks(
        [b[images:mod_base] for b in blocks],
        [b[mod_base + 2 : mod_base + 4] for b in blocks],
        width,
    )

    half = local_width // 2
    swap = [(0, 1), (1, 0)]

    def own_half(weight, axis):
        return lax.dynamic_slice_in_dim(weight, core * half, half, axis=axis)

    txt_w = lax.all_gather(own_half(txt_kv_weight, 2), "col", axis=0, tiled=True)
    img_w = lax.all_gather(own_half(img_qkv_weight, 2), "col", axis=0, tiled=True)
    out_w = lax.all_gather(own_half(out_weight, 0), "col", axis=1, tiled=True)
    halves = [
        (txt_w, img_w, out_w),
        tuple(lax.ppermute(w, "cfg", swap) for w in (txt_w, img_w, out_w)),
    ]
    positions = jnp.arange(text_slots + images, dtype=jnp.int32)
    usable = (positions < txt_len[0, 0]) | (positions >= text_slots)
    heads_half = half // HD

    def attend(txt_w, img_w, out_w):
        img_proj = add_rows(img_w, img_ready).reshape(images, 3, heads_half, HD)
        txt_proj = add_rows(txt_w, txt_ready).reshape(text_slots, 2, heads_half, HD)
        queries = rms_norm(img_proj[:, 0]).astype(jnp.bfloat16)
        key_rows = jnp.concatenate(
            [rms_norm(txt_proj[:, 0]), rms_norm(img_proj[:, 1])], 0
        ).astype(jnp.bfloat16)
        value_rows = jnp.concatenate([txt_proj[:, 1], img_proj[:, 2]], 0).astype(jnp.bfloat16)
        scores = jnp.einsum(
            "qhe,khe->hqk", queries, key_rows, preferred_element_type=jnp.float32
        ) / math.sqrt(HD)
        weights = jnp.where(usable, jnp.exp(scores), 0.0)
        chances = (weights / jnp.sum(weights, -1, keepdims=True)).astype(jnp.bfloat16)
        mixed = jnp.einsum("hqk,khe->qhe", chances, value_rows, preferred_element_type=jnp.float32)
        outputs = mixed.reshape(images, half).astype(jnp.bfloat16)
        return jnp.einsum(
            "ti,iko->kto",
            outputs,
            out_w.reshape(half, n_row, local_width),
            preferred_element_type=jnp.float32,
        )

    term_blocks = (attend(*halves[0]) + attend(*halves[1])).astype(jnp.bfloat16)
    projected = lax.dynamic_index_in_dim(term_blocks, me_row, 0, keepdims=False).astype(jnp.float32)
    for step in range(1, n_row):
        outgoing = lax.dynamic_index_in_dim(term_blocks, (me_row + step) % n_row, 0, keepdims=False)
        projected = projected + lax.ppermute(outgoing, "row", shift_pairs(n_row, step)).astype(
            jnp.float32
        )
    gating = img_gate[0].astype(jnp.float32)
    img_out = (img_tokens[0, 0].astype(jnp.float32) + gating * projected).astype(jnp.bfloat16)
    velocity = jnp.dot(img_out, final_weight, preferred_element_type=jnp.float32)
    strength = guidance[0]
    share = jnp.where(core == 1, strength, 1.0 - strength)
    weighted = velocity * share
    n_pair = 2 * n_row
    me_pair = core * n_row + me_row
    rows_each = weighted.shape[0] // n_pair
    velocity_blocks = weighted.reshape(n_pair, rows_each, weighted.shape[1])
    guided = lax.dynamic_index_in_dim(velocity_blocks, me_pair, 0, keepdims=False)
    for step in range(1, n_pair):
        outgoing = lax.dynamic_index_in_dim(velocity_blocks, (me_pair + step) % n_pair, 0, keepdims=False)
        guided = guided + lax.ppermute(outgoing, ("cfg", "row"), shift_pairs(n_pair, step))
    position_now = step_index[0]
    step_size = sigmas[position_now + 1] - sigmas[position_now]
    return (img_out[None, None], latent + step_size * guided[None])


def solution(mesh):
    return jax.shard_map(
        shards,
        mesh=mesh,
        in_specs=(
            P("cfg", "col", None, "row"),
            P("cfg", "col", None, "row"),
            P("cfg", "col", None, "row"),
            P("cfg", "col", None, "row"),
            P("cfg", "col", "row"),
            P("cfg", "col"),
            P("col", None, "row"),
            P("col", None, "row"),
            P("row", "col"),
            P("row", None),
            P("col", ("cfg", "row"), None),
            P(),
            P(),
            P(),
        ),
        out_specs=(P("cfg", "col", None, "row"), P("col", ("cfg", "row"), None)),
        check_vma=False,
    )
```

```python
import math

import jax
import jax.numpy as jnp
from jax import lax
from jax.sharding import PartitionSpec as P

HD = 128


def rms_norm(values):
    return values * lax.rsqrt(jnp.mean(values * values, -1, keepdims=True) + 1e-06)


def shift_pairs(size, step):
    return [(i, (i + step) % size) for i in range(size)]


def ring_gather(piece, axis_name, size):
    assert size == 4
    from_prev = lax.ppermute(piece, axis_name, shift_pairs(size, 1))
    from_next = lax.ppermute(piece, axis_name, shift_pairs(size, -1))
    cut = piece.shape[0] // 2
    far_top = lax.ppermute(from_prev[:cut], axis_name, shift_pairs(size, 1))
    far_bottom = lax.ppermute(from_next[cut:], axis_name, shift_pairs(size, -1))
    far = jnp.concatenate([far_top, far_bottom], 0)
    return [piece, from_next, far, from_prev]


def modulate_blocks(blocks, mods, width):
    values = [b.astype(jnp.float32) for b in blocks]
    mean = sum(jnp.sum(v, -1, keepdims=True) for v in values) / width
    centred = [v - mean for v in values]
    spread = sum(jnp.sum(c * c, -1, keepdims=True) for c in centred) / width
    scale = lax.rsqrt(spread + 1e-06)
    out = []
    for c, m in zip(centred, mods):
        m = m.astype(jnp.float32)
        out.append(((c * scale) * (1.0 + m[1:2]) + m[0:1]).astype(jnp.bfloat16))
    return jnp.concatenate(out, -1)


def order_blocks(by_offset, me, size):
    stacked = jnp.stack(by_offset)
    return [
        lax.dynamic_index_in_dim(stacked, (k - me) % size, 0, keepdims=False) for k in range(size)
    ]


def add_rows(piece, ready):
    return jnp.dot(ready, piece.reshape(piece.shape[0], -1), preferred_element_type=jnp.float32)


def shards(
    img_tokens,
    txt_tokens,
    img_mod,
    txt_mod,
    img_gate,
    txt_len,
    img_qkv_weight,
    txt_kv_weight,
    out_weight,
    final_weight,
    latent,
    sigmas,
    step_index,
    guidance,
):
    n_row = 4
    images = img_tokens.shape[2]
    text_slots = txt_tokens.shape[2]
    local_width = img_qkv_weight.shape[2]
    width = local_width * n_row
    heads_here = local_width // HD
    me_row = lax.axis_index("row")
    core = lax.axis_index("cfg")

    img_blocks = order_blocks(ring_gather(img_tokens[0, 0], "row", n_row), me_row, n_row)
    txt_bundle = jnp.concatenate([txt_tokens[0, 0], img_mod[0, 0], txt_mod[0, 0]], 0)
    txt_blocks = order_blocks(ring_gather(txt_bundle, "row", n_row), me_row, n_row)
    img_ready = modulate_blocks(
        img_blocks, [b[text_slots : text_slots + 2] for b in txt_blocks], width
    )
    txt_ready = modulate_blocks(
        [b[:text_slots] for b in txt_blocks],
        [b[text_slots + 2 : text_slots + 4] for b in txt_blocks],
        width,
    )
    half = local_width // 2
    swap = [(0, 1), (1, 0)]

    def own_half(weight, axis):
        return lax.dynamic_slice_in_dim(weight, core * half, half, axis=axis)

    img_w = lax.all_gather(own_half(img_qkv_weight, 2), "col", axis=0, tiled=True)
    img_w, txt_piece = lax.optimization_barrier((img_w, own_half(txt_kv_weight, 2)))
    txt_w = lax.all_gather(txt_piece, "col", axis=0, tiled=True)
    txt_w, out_piece = lax.optimization_barrier((txt_w, own_half(out_weight, 0)))
    out_w = lax.all_gather(out_piece, "col", axis=1, tiled=True)
    halves = [
        (txt_w, img_w, out_w),
        tuple(lax.ppermute(w, "cfg", swap) for w in (txt_w, img_w, out_w)),
    ]
    positions = jnp.arange(text_slots + images, dtype=jnp.int32)
    usable = (positions < txt_len[0, 0]) | (positions >= text_slots)
    heads_half = half // HD

    def project(txt_w, img_w):
        img_proj = add_rows(img_w, img_ready).reshape(images, 3, heads_half, HD)
        txt_proj = add_rows(txt_w, txt_ready).reshape(text_slots, 2, heads_half, HD)
        queries = rms_norm(img_proj[:, 0]).astype(jnp.bfloat16)
        key_rows = jnp.concatenate(
            [rms_norm(txt_proj[:, 0]), rms_norm(img_proj[:, 1])], 0
        ).astype(jnp.bfloat16)
        value_rows = jnp.concatenate([txt_proj[:, 1], img_proj[:, 2]], 0).astype(jnp.bfloat16)
        return queries, key_rows, value_rows

    def attend(queries, key_rows, value_rows, out_w):
        scores = jnp.einsum(
            "qhe,khe->hqk", queries, key_rows, preferred_element_type=jnp.float32
        ) / math.sqrt(HD)
        weights = jnp.where(usable, jnp.exp(scores), 0.0)
        chances = (weights / jnp.sum(weights, -1, keepdims=True)).astype(jnp.bfloat16)
        mixed = jnp.einsum("hqk,khe->qhe", chances, value_rows, preferred_element_type=jnp.float32)
        outputs = mixed.reshape(queries.shape[0], half).astype(jnp.bfloat16)
        return jnp.einsum(
            "ti,iko->kto",
            outputs,
            out_w.reshape(half, n_row, local_width),
            preferred_element_type=jnp.float32,
        )

    projections = [project(*h[:2]) for h in halves]
    n_chunk = 2
    chunk = images // n_chunk
    pieces = []
    for c in range(n_chunk):
        part = 0.0
        for (queries, key_rows, value_rows), h in zip(projections, halves):
            part = part + attend(queries[c * chunk : (c + 1) * chunk], key_rows, value_rows, h[2])
        term_blocks = part.astype(jnp.bfloat16)
        got = lax.dynamic_index_in_dim(term_blocks, me_row, 0, keepdims=False).astype(jnp.float32)
        for step in range(1, n_row):
            outgoing = lax.dynamic_index_in_dim(term_blocks, (me_row + step) % n_row, 0, keepdims=False)
            got = got + lax.ppermute(outgoing, "row", shift_pairs(n_row, step)).astype(jnp.float32)
        pieces.append(got)
    projected = jnp.concatenate(pieces, 0)
    gating = img_gate[0].astype(jnp.float32)
    img_out = (img_tokens[0, 0].astype(jnp.float32) + gating * projected).astype(jnp.bfloat16)
    velocity = jnp.dot(img_out, final_weight, preferred_element_type=jnp.float32)
    strength = guidance[0]
    share = jnp.where(core == 1, strength, 1.0 - strength)
    weighted = velocity * share
    n_pair = 2 * n_row
    me_pair = core * n_row + me_row
    rows_each = weighted.shape[0] // n_pair
    velocity_blocks = weighted.reshape(n_pair, rows_each, weighted.shape[1])
    guided = lax.dynamic_index_in_dim(velocity_blocks, me_pair, 0, keepdims=False)
    for step in range(1, n_pair):
        outgoing = lax.dynamic_index_in_dim(velocity_blocks, (me_pair + step) % n_pair, 0, keepdims=False)
        guided = guided + lax.ppermute(outgoing, ("cfg", "row"), shift_pairs(n_pair, step))
    position_now = step_index[0]
    step_size = sigmas[position_now + 1] - sigmas[position_now]
    return (img_out[None, None], latent + step_size * guided[None])


def solution(mesh):
    return jax.shard_map(
        shards,
        mesh=mesh,
        in_specs=(
            P("cfg", "col", None, "row"),
            P("cfg", "col", None, "row"),
            P("cfg", "col", None, "row"),
            P("cfg", "col", None, "row"),
            P("cfg", "col", "row"),
            P("cfg", "col"),
            P("col", None, "row"),
            P("col", None, "row"),
            P("row", "col"),
            P("row", None),
            P("col", ("cfg", "row"), None),
            P(),
            P(),
            P(),
        ),
        out_specs=(P("cfg", "col", None, "row"), P("col", ("cfg", "row"), None)),
        check_vma=False,
    )
```

```python
import math

import jax
import jax.numpy as jnp
from jax import lax
from jax.sharding import PartitionSpec as P


HD = 128


def rms_norm(values):
    return values * lax.rsqrt(jnp.mean(values * values, -1, keepdims=True) + 1e-06)


def shift_pairs(size, step):
    return [(i, (i + step) % size) for i in range(size)]


def ring_gather(piece, axis_name, size):
    assert size == 4
    from_prev = lax.ppermute(piece, axis_name, shift_pairs(size, 1))
    from_next = lax.ppermute(piece, axis_name, shift_pairs(size, -1))
    cut = piece.shape[0] // 2
    far_top = lax.ppermute(from_prev[:cut], axis_name, shift_pairs(size, 1))
    far_bottom = lax.ppermute(from_next[cut:], axis_name, shift_pairs(size, -1))
    far = jnp.concatenate([far_top, far_bottom], 0)
    return [piece, from_next, far, from_prev]


def modulate_blocks(blocks, mods, width):
    values = [b.astype(jnp.float32) for b in blocks]
    mean = sum(jnp.sum(v, -1, keepdims=True) for v in values) / width
    centred = [v - mean for v in values]
    spread = sum(jnp.sum(c * c, -1, keepdims=True) for c in centred) / width
    scale = lax.rsqrt(spread + 1e-06)
    out = []
    for c, m in zip(centred, mods):
        m = m.astype(jnp.float32)
        out.append(((c * scale) * (1.0 + m[1:2]) + m[0:1]).astype(jnp.bfloat16))
    return jnp.concatenate(out, -1)


def order_blocks(by_offset, me, size):
    stacked = jnp.stack(by_offset)
    return [
        lax.dynamic_index_in_dim(stacked, (k - me) % size, 0, keepdims=False) for k in range(size)
    ]


def add_rows(piece, ready):
    return jnp.dot(ready, piece.reshape(piece.shape[0], -1), preferred_element_type=jnp.float32)


def layer(
    img_tokens,
    txt_tokens,
    img_mod,
    txt_mod,
    img_gate,
    txt_len,
    img_qkv_weight,
    txt_kv_weight,
    out_weight,
    final_weight,
    latent,
    sigmas,
    step_index,
    guidance,
):
    n_row = 4
    images = img_tokens.shape[2]
    text_slots = txt_tokens.shape[2]
    local_width = img_qkv_weight.shape[2]
    width = local_width * n_row
    me_row = lax.axis_index("row")
    core = lax.axis_index("cfg")

    img_blocks = order_blocks(ring_gather(img_tokens[0, 0], "row", n_row), me_row, n_row)
    txt_bundle = jnp.concatenate([txt_tokens[0, 0], img_mod[0, 0], txt_mod[0, 0]], 0)
    txt_blocks = order_blocks(ring_gather(txt_bundle, "row", n_row), me_row, n_row)
    img_ready = modulate_blocks(
        img_blocks, [b[text_slots : text_slots + 2] for b in txt_blocks], width
    )
    txt_ready = modulate_blocks(
        [b[:text_slots] for b in txt_blocks],
        [b[text_slots + 2 : text_slots + 4] for b in txt_blocks],
        width,
    )
    half = local_width // 2
    swap = [(0, 1), (1, 0)]

    def own_half(weight, axis):
        return lax.dynamic_slice_in_dim(weight, core * half, half, axis=axis)

    img_w = lax.all_gather(own_half(img_qkv_weight, 2), "col", axis=0, tiled=True)
    rows_here = txt_kv_weight.shape[0]
    txt_out_piece = jnp.concatenate(
        [own_half(txt_kv_weight, 2).reshape(rows_here, -1), own_half(out_weight, 0).T], 1
    )
    img_w, txt_out_piece = lax.optimization_barrier((img_w, txt_out_piece))
    txt_out_w = lax.all_gather(txt_out_piece, "col", axis=0, tiled=True)
    txt_w = txt_out_w[:, : 2 * half].reshape(width, 2, half)
    out_w = txt_out_w[:, 2 * half :].T
    img_w_other = lax.ppermute(img_w, "cfg", swap)
    halves = [
        (txt_w, img_w, out_w),
        (lax.ppermute(txt_w, "cfg", swap), img_w_other, lax.ppermute(out_w, "cfg", swap)),
    ]
    positions = jnp.arange(text_slots + images, dtype=jnp.int32)
    usable = (positions < txt_len[0, 0]) | (positions >= text_slots)
    heads_half = half // HD

    def project(txt_w, img_w):
        img_proj = add_rows(img_w, img_ready).reshape(images, 3, heads_half, HD)
        txt_proj = add_rows(txt_w, txt_ready).reshape(text_slots, 2, heads_half, HD)
        queries = rms_norm(img_proj[:, 0]).astype(jnp.bfloat16)
        key_rows = jnp.concatenate(
            [rms_norm(txt_proj[:, 0]), rms_norm(img_proj[:, 1])], 0
        ).astype(jnp.bfloat16)
        value_rows = jnp.concatenate([txt_proj[:, 1], img_proj[:, 2]], 0).astype(jnp.bfloat16)
        return queries, key_rows, value_rows

    def attend(queries, key_rows, value_rows, out_w):
        scores = jnp.einsum(
            "qhe,khe->hqk", queries, key_rows, preferred_element_type=jnp.float32
        ) / math.sqrt(HD)
        weights = jnp.where(usable, jnp.exp(scores), 0.0)
        chances = (weights / jnp.sum(weights, -1, keepdims=True)).astype(jnp.bfloat16)
        mixed = jnp.einsum("hqk,khe->qhe", chances, value_rows, preferred_element_type=jnp.float32)
        outputs = mixed.reshape(queries.shape[0], half).astype(jnp.bfloat16)
        return jnp.einsum(
            "ti,iko->kto",
            outputs,
            out_w.reshape(half, n_row, local_width),
            preferred_element_type=jnp.float32,
        )

    projections = [project(*h[:2]) for h in halves]
    n_chunk = 2
    chunk = images // n_chunk
    pieces = []
    for c in range(n_chunk):
        part = 0.0
        for (queries, key_rows, value_rows), h in zip(projections, halves):
            part = part + attend(queries[c * chunk : (c + 1) * chunk], key_rows, value_rows, h[2])
        term_blocks = part.astype(jnp.bfloat16)
        got = lax.dynamic_index_in_dim(term_blocks, me_row, 0, keepdims=False).astype(jnp.float32)
        for step in range(1, n_row):
            outgoing = lax.dynamic_index_in_dim(term_blocks, (me_row + step) % n_row, 0, keepdims=False)
            got = got + lax.ppermute(outgoing, "row", shift_pairs(n_row, step)).astype(jnp.float32)
        pieces.append(got)
    projected = jnp.concatenate(pieces, 0)
    gating = img_gate[0].astype(jnp.float32)
    img_out = (img_tokens[0, 0].astype(jnp.float32) + gating * projected).astype(jnp.bfloat16)
    velocity = jnp.dot(img_out, final_weight, preferred_element_type=jnp.float32)
    strength = guidance[0]
    share = jnp.where(core == 1, strength, 1.0 - strength)
    weighted = velocity * share
    n_pair = 2 * n_row
    me_pair = core * n_row + me_row
    rows_each = weighted.shape[0] // n_pair
    velocity_blocks = weighted.reshape(n_pair, rows_each, weighted.shape[1])
    guided = lax.dynamic_index_in_dim(velocity_blocks, me_pair, 0, keepdims=False)
    for step in range(1, n_pair):
        outgoing = lax.dynamic_index_in_dim(velocity_blocks, (me_pair + step) % n_pair, 0, keepdims=False)
        guided = guided + lax.ppermute(outgoing, ("cfg", "row"), shift_pairs(n_pair, step))
    position_now = step_index[0]
    step_size = sigmas[position_now + 1] - sigmas[position_now]
    return (img_out[None, None], latent + step_size * guided[None])


def solution(mesh):
    return jax.shard_map(
        layer,
        mesh=mesh,
        in_specs=(
            P("cfg", "col", None, "row"),
            P("cfg", "col", None, "row"),
            P("cfg", "col", None, "row"),
            P("cfg", "col", None, "row"),
            P("cfg", "col", "row"),
            P("cfg", "col"),
            P("col", None, "row"),
            P("col", None, "row"),
            P("row", "col"),
            P("row", None),
            P("col", ("cfg", "row"), None),
            P(),
            P(),
            P(),
        ),
        out_specs=(P("cfg", "col", None, "row"), P("col", ("cfg", "row"), None)),
        check_vma=False,
    )
```

```python
import math

import jax
import jax.numpy as jnp
from jax import lax
from jax.sharding import PartitionSpec as P


HD = 128


def rms_norm(values):
    return values * lax.rsqrt(jnp.mean(values * values, -1, keepdims=True) + 1e-06)


def shift_pairs(size, step):
    return [(i, (i + step) % size) for i in range(size)]


def ring_gather(piece, axis_name, size):
    assert size == 4
    from_prev = lax.ppermute(piece, axis_name, shift_pairs(size, 1))
    from_next = lax.ppermute(piece, axis_name, shift_pairs(size, -1))
    cut = piece.shape[0] // 2
    far_top = lax.ppermute(from_prev[:cut], axis_name, shift_pairs(size, 1))
    far_bottom = lax.ppermute(from_next[cut:], axis_name, shift_pairs(size, -1))
    far = jnp.concatenate([far_top, far_bottom], 0)
    return [piece, from_next, far, from_prev]


def modulate_blocks(blocks, mods, width):
    values = [b.astype(jnp.float32) for b in blocks]
    mean = sum(jnp.sum(v, -1, keepdims=True) for v in values) / width
    centred = [v - mean for v in values]
    spread = sum(jnp.sum(c * c, -1, keepdims=True) for c in centred) / width
    scale = lax.rsqrt(spread + 1e-06)
    out = []
    for c, m in zip(centred, mods):
        m = m.astype(jnp.float32)
        out.append(((c * scale) * (1.0 + m[1:2]) + m[0:1]).astype(jnp.bfloat16))
    return jnp.concatenate(out, -1)


def order_blocks(by_offset, me, size):
    stacked = jnp.stack(by_offset)
    return [
        lax.dynamic_index_in_dim(stacked, (k - me) % size, 0, keepdims=False) for k in range(size)
    ]


def add_rows(piece, ready):
    return jnp.einsum("ti,sin->tsn", ready, piece, preferred_element_type=jnp.float32)


def layer(
    img_tokens,
    txt_tokens,
    img_mod,
    txt_mod,
    img_gate,
    txt_len,
    img_qkv_weight,
    txt_kv_weight,
    out_weight,
    final_weight,
    latent,
    sigmas,
    step_index,
    guidance,
):
    n_row = 4
    images = img_tokens.shape[2]
    text_slots = txt_tokens.shape[2]
    local_width = img_qkv_weight.shape[2]
    width = local_width * n_row
    me_row = lax.axis_index("row")
    core = lax.axis_index("cfg")

    img_blocks = order_blocks(ring_gather(img_tokens[0, 0], "row", n_row), me_row, n_row)
    txt_bundle = jnp.concatenate([txt_tokens[0, 0], img_mod[0, 0], txt_mod[0, 0]], 0)
    txt_blocks = order_blocks(ring_gather(txt_bundle, "row", n_row), me_row, n_row)
    img_ready = modulate_blocks(
        img_blocks, [b[text_slots : text_slots + 2] for b in txt_blocks], width
    )
    txt_ready = modulate_blocks(
        [b[:text_slots] for b in txt_blocks],
        [b[text_slots + 2 : text_slots + 4] for b in txt_blocks],
        width,
    )
    half = local_width // 2
    swap = [(0, 1), (1, 0)]

    def own_half(weight, axis):
        return lax.dynamic_slice_in_dim(weight, core * half, half, axis=axis)

    img_piece = jnp.transpose(own_half(img_qkv_weight, 2), (1, 0, 2))
    img_w = lax.all_gather(img_piece, "col", axis=1, tiled=True)
    txt_out_piece = jnp.concatenate(
        [jnp.transpose(own_half(txt_kv_weight, 2), (1, 0, 2)), own_half(out_weight, 0).T[None]], 0
    )
    img_w, txt_out_piece = lax.optimization_barrier((img_w, txt_out_piece))
    txt_out_w = lax.all_gather(txt_out_piece, "col", axis=1, tiled=True)
    txt_w = txt_out_w[:2]
    out_w = txt_out_w[2]
    img_w_other = lax.ppermute(img_w, "cfg", swap)
    halves = [
        (txt_w, img_w, out_w),
        (lax.ppermute(txt_w, "cfg", swap), img_w_other, lax.ppermute(out_w, "cfg", swap)),
    ]
    positions = jnp.arange(text_slots + images, dtype=jnp.int32)
    usable = (positions < txt_len[0, 0]) | (positions >= text_slots)
    heads_half = half // HD

    def project(txt_w, img_w):
        img_proj = add_rows(img_w, img_ready).reshape(images, 3, heads_half, HD)
        txt_proj = add_rows(txt_w, txt_ready).reshape(text_slots, 2, heads_half, HD)
        queries = rms_norm(img_proj[:, 0]).astype(jnp.bfloat16)
        key_rows = jnp.concatenate(
            [rms_norm(txt_proj[:, 0]), rms_norm(img_proj[:, 1])], 0
        ).astype(jnp.bfloat16)
        value_rows = jnp.concatenate([txt_proj[:, 1], img_proj[:, 2]], 0).astype(jnp.bfloat16)
        return queries, key_rows, value_rows

    def attend(queries, key_rows, value_rows, out_w):
        scores = jnp.einsum(
            "qhe,khe->hqk", queries, key_rows, preferred_element_type=jnp.float32
        ) / math.sqrt(HD)
        weights = jnp.where(usable, jnp.exp(scores), 0.0)
        chances = (weights / jnp.sum(weights, -1, keepdims=True)).astype(jnp.bfloat16)
        mixed = jnp.einsum("hqk,khe->qhe", chances, value_rows, preferred_element_type=jnp.float32)
        outputs = mixed.reshape(queries.shape[0], half).astype(jnp.bfloat16)
        return jnp.einsum(
            "ti,koi->kto",
            outputs,
            out_w.reshape(n_row, local_width, half),
            preferred_element_type=jnp.float32,
        )

    projections = [project(*h[:2]) for h in halves]
    n_chunk = 2
    chunk = images // n_chunk
    pieces = []
    for c in range(n_chunk):
        part = 0.0
        for (queries, key_rows, value_rows), h in zip(projections, halves):
            part = part + attend(queries[c * chunk : (c + 1) * chunk], key_rows, value_rows, h[2])
        term_blocks = part.astype(jnp.bfloat16)
        got = lax.dynamic_index_in_dim(term_blocks, me_row, 0, keepdims=False).astype(jnp.float32)
        for step in range(1, n_row):
            outgoing = lax.dynamic_index_in_dim(
                term_blocks, (me_row + step) % n_row, 0, keepdims=False
            )
            got = got + lax.ppermute(outgoing, "row", shift_pairs(n_row, step)).astype(jnp.float32)
        pieces.append(got)
    projected = jnp.concatenate(pieces, 0)
    gating = img_gate[0].astype(jnp.float32)
    img_out = (img_tokens[0, 0].astype(jnp.float32) + gating * projected).astype(jnp.bfloat16)
    velocity = jnp.dot(img_out, final_weight, preferred_element_type=jnp.float32)
    strength = guidance[0]
    share = jnp.where(core == 1, strength, 1.0 - strength)
    weighted = velocity * share
    n_pair = 2 * n_row
    me_pair = core * n_row + me_row
    rows_each = weighted.shape[0] // n_pair
    velocity_blocks = weighted.reshape(n_pair, rows_each, weighted.shape[1])
    guided = lax.dynamic_index_in_dim(velocity_blocks, me_pair, 0, keepdims=False)
    for step in range(1, n_pair):
        outgoing = lax.dynamic_index_in_dim(velocity_blocks, (me_pair + step) % n_pair, 0, keepdims=False)
        guided = guided + lax.ppermute(outgoing, ("cfg", "row"), shift_pairs(n_pair, step))
    position_now = step_index[0]
    step_size = sigmas[position_now + 1] - sigmas[position_now]
    return (img_out[None, None], latent + step_size * guided[None])


def solution(mesh):
    return jax.shard_map(
        layer,
        mesh=mesh,
        in_specs=(
            P("cfg", "col", None, "row"),
            P("cfg", "col", None, "row"),
            P("cfg", "col", None, "row"),
            P("cfg", "col", None, "row"),
            P("cfg", "col", "row"),
            P("cfg", "col"),
            P("col", None, "row"),
            P("col", None, "row"),
            P("row", "col"),
            P("row", None),
            P("col", ("cfg", "row"), None),
            P(),
            P(),
            P(),
        ),
        out_specs=(P("cfg", "col", None, "row"), P("col", ("cfg", "row"), None)),
        check_vma=False,
    )
```

```python
import math

import jax
import jax.numpy as jnp
from jax import lax
from jax.sharding import PartitionSpec as P


HD = 128


def rms_norm(values):
    return values * lax.rsqrt(jnp.mean(values * values, -1, keepdims=True) + 1e-06)


def shift_pairs(size, step):
    return [(i, (i + step) % size) for i in range(size)]


def ring_gather(piece, axis_name, size):
    assert size == 4
    from_prev = lax.ppermute(piece, axis_name, shift_pairs(size, 1))
    from_next = lax.ppermute(piece, axis_name, shift_pairs(size, -1))
    cut = piece.shape[0] // 2
    far_top = lax.ppermute(from_prev[:cut], axis_name, shift_pairs(size, 1))
    far_bottom = lax.ppermute(from_next[cut:], axis_name, shift_pairs(size, -1))
    far = jnp.concatenate([far_top, far_bottom], 0)
    return [piece, from_next, far, from_prev]


def reduce_blocks(term_blocks, me, axis_name, size):
    assert size == 4
    rows = term_blocks.shape[1]
    cut = rows // 2

    def block(offset):
        return lax.dynamic_index_in_dim(term_blocks, (me + offset) % size, 0, keepdims=False)

    far = block(2)
    up = lax.ppermute(jnp.concatenate([block(1), far[:cut]], 0), axis_name, shift_pairs(size, 1))
    down = lax.ppermute(
        jnp.concatenate([block(-1), far[cut:]], 0), axis_name, shift_pairs(size, -1)
    )
    far_top = lax.ppermute(up[rows:], axis_name, shift_pairs(size, 1))
    far_bottom = lax.ppermute(down[rows:], axis_name, shift_pairs(size, -1))
    got = block(0).astype(jnp.float32) + up[:rows].astype(jnp.float32)
    got = got + down[:rows].astype(jnp.float32)
    return got + jnp.concatenate([far_top, far_bottom], 0).astype(jnp.float32)


def modulate_blocks(blocks, mods, width):
    values = [b.astype(jnp.float32) for b in blocks]
    mean = sum(jnp.sum(v, -1, keepdims=True) for v in values) / width
    centred = [v - mean for v in values]
    spread = sum(jnp.sum(c * c, -1, keepdims=True) for c in centred) / width
    scale = lax.rsqrt(spread + 1e-06)
    out = []
    for c, m in zip(centred, mods):
        m = m.astype(jnp.float32)
        out.append(((c * scale) * (1.0 + m[1:2]) + m[0:1]).astype(jnp.bfloat16))
    return jnp.concatenate(out, -1)


def order_blocks(by_offset, me, size):
    stacked = jnp.stack(by_offset)
    return [
        lax.dynamic_index_in_dim(stacked, (k - me) % size, 0, keepdims=False) for k in range(size)
    ]


def add_rows(piece, ready):
    return jnp.einsum("ti,sin->tsn", ready, piece, preferred_element_type=jnp.float32)


def layer(
    img_tokens,
    txt_tokens,
    img_mod,
    txt_mod,
    img_gate,
    txt_len,
    img_qkv_weight,
    txt_kv_weight,
    out_weight,
    final_weight,
    latent,
    sigmas,
    step_index,
    guidance,
):
    n_row = 4
    images = img_tokens.shape[2]
    text_slots = txt_tokens.shape[2]
    local_width = img_qkv_weight.shape[2]
    width = local_width * n_row
    me_row = lax.axis_index("row")
    core = lax.axis_index("cfg")

    img_blocks = order_blocks(ring_gather(img_tokens[0, 0], "row", n_row), me_row, n_row)
    txt_bundle = jnp.concatenate([txt_tokens[0, 0], img_mod[0, 0], txt_mod[0, 0]], 0)
    txt_blocks = order_blocks(ring_gather(txt_bundle, "row", n_row), me_row, n_row)
    img_ready = modulate_blocks(
        img_blocks, [b[text_slots : text_slots + 2] for b in txt_blocks], width
    )
    txt_ready = modulate_blocks(
        [b[:text_slots] for b in txt_blocks],
        [b[text_slots + 2 : text_slots + 4] for b in txt_blocks],
        width,
    )
    half = local_width // 2
    swap = [(0, 1), (1, 0)]

    def own_half(weight, axis):
        return lax.dynamic_slice_in_dim(weight, core * half, half, axis=axis)

    img_piece = jnp.transpose(own_half(img_qkv_weight, 2), (1, 0, 2))
    img_w = lax.all_gather(img_piece, "col", axis=1, tiled=True)
    txt_out_piece = jnp.concatenate(
        [jnp.transpose(own_half(txt_kv_weight, 2), (1, 0, 2)), own_half(out_weight, 0).T[None]], 0
    )
    img_w, txt_out_piece = lax.optimization_barrier((img_w, txt_out_piece))
    txt_out_w = lax.all_gather(txt_out_piece, "col", axis=1, tiled=True)
    txt_w = txt_out_w[:2]
    out_w = txt_out_w[2]
    img_w_other = lax.ppermute(img_w, "cfg", swap)
    txt_out_other = lax.ppermute(txt_out_w, "cfg", swap)
    halves = [
        (txt_w, img_w, out_w),
        (txt_out_other[:2], img_w_other, txt_out_other[2]),
    ]
    positions = jnp.arange(text_slots + images, dtype=jnp.int32)
    usable = (positions < txt_len[0, 0]) | (positions >= text_slots)
    heads_half = half // HD

    def project(txt_w, img_w):
        img_proj = add_rows(img_w, img_ready).reshape(images, 3, heads_half, HD)
        txt_proj = add_rows(txt_w, txt_ready).reshape(text_slots, 2, heads_half, HD)
        queries = rms_norm(img_proj[:, 0]).astype(jnp.bfloat16)
        key_rows = jnp.concatenate(
            [rms_norm(txt_proj[:, 0]), rms_norm(img_proj[:, 1])], 0
        ).astype(jnp.bfloat16)
        value_rows = jnp.concatenate([txt_proj[:, 1], img_proj[:, 2]], 0).astype(jnp.bfloat16)
        return queries, key_rows, value_rows

    def attend(queries, key_rows, value_rows, out_w):
        scores = jnp.einsum(
            "qhe,khe->hqk", queries, key_rows, preferred_element_type=jnp.float32
        ) / math.sqrt(HD)
        weights = jnp.where(usable, jnp.exp(scores), 0.0)
        chances = (weights / jnp.sum(weights, -1, keepdims=True)).astype(jnp.bfloat16)
        mixed = jnp.einsum("hqk,khe->qhe", chances, value_rows, preferred_element_type=jnp.float32)
        outputs = mixed.reshape(queries.shape[0], half).astype(jnp.bfloat16)
        return jnp.einsum(
            "ti,koi->kto",
            outputs,
            out_w.reshape(n_row, local_width, half),
            preferred_element_type=jnp.float32,
        )

    projections = [project(*h[:2]) for h in halves]
    n_chunk = 2
    chunk = images // n_chunk
    pieces = []
    for c in range(n_chunk):
        part = 0.0
        for (queries, key_rows, value_rows), h in zip(projections, halves):
            part = part + attend(queries[c * chunk : (c + 1) * chunk], key_rows, value_rows, h[2])
        term_blocks = part.astype(jnp.bfloat16)
        got = reduce_blocks(term_blocks, me_row, "row", n_row)
        pieces.append(got)
    projected = jnp.concatenate(pieces, 0)
    gating = img_gate[0].astype(jnp.float32)
    img_out = (img_tokens[0, 0].astype(jnp.float32) + gating * projected).astype(jnp.bfloat16)
    velocity = jnp.dot(img_out, final_weight, preferred_element_type=jnp.float32)
    strength = guidance[0]
    share = jnp.where(core == 1, strength, 1.0 - strength)
    weighted = velocity * share
    n_pair = 2 * n_row
    me_pair = core * n_row + me_row
    rows_each = weighted.shape[0] // n_pair
    velocity_blocks = weighted.reshape(n_pair, rows_each, weighted.shape[1])
    guided = lax.dynamic_index_in_dim(velocity_blocks, me_pair, 0, keepdims=False)
    for step in range(1, n_pair):
        outgoing = lax.dynamic_index_in_dim(velocity_blocks, (me_pair + step) % n_pair, 0, keepdims=False)
        guided = guided + lax.ppermute(outgoing, ("cfg", "row"), shift_pairs(n_pair, step))
    position_now = step_index[0]
    step_size = sigmas[position_now + 1] - sigmas[position_now]
    return (img_out[None, None], latent + step_size * guided[None])


def solution(mesh):
    return jax.shard_map(
        layer,
        mesh=mesh,
        in_specs=(
            P("cfg", "col", None, "row"),
            P("cfg", "col", None, "row"),
            P("cfg", "col", None, "row"),
            P("cfg", "col", None, "row"),
            P("cfg", "col", "row"),
            P("cfg", "col"),
            P("col", None, "row"),
            P("col", None, "row"),
            P("row", "col"),
            P("row", None),
            P("col", ("cfg", "row"), None),
            P(),
            P(),
            P(),
        ),
        out_specs=(P("cfg", "col", None, "row"), P("col", ("cfg", "row"), None)),
        check_vma=False,
    )
```

```python
import math

import jax
import jax.numpy as jnp
from jax import lax
from jax.sharding import PartitionSpec as P


HD = 128


def rms_norm(values):
    return values * lax.rsqrt(jnp.mean(values * values, -1, keepdims=True) + 1e-06)


def shift_pairs(size, step):
    return [(i, (i + step) % size) for i in range(size)]


def ring_gather(piece, axis_name, size):
    assert size == 4
    from_prev = lax.ppermute(piece, axis_name, shift_pairs(size, 1))
    from_next = lax.ppermute(piece, axis_name, shift_pairs(size, -1))
    cut = piece.shape[0] // 2
    far_top = lax.ppermute(from_prev[:cut], axis_name, shift_pairs(size, 1))
    far_bottom = lax.ppermute(from_next[cut:], axis_name, shift_pairs(size, -1))
    far = jnp.concatenate([far_top, far_bottom], 0)
    return [piece, from_next, far, from_prev]


def reduce_blocks(term_blocks, me, axis_name, size):
    assert size == 4
    rows = term_blocks.shape[1]
    cut = rows // 2

    def block(offset):
        return lax.dynamic_index_in_dim(term_blocks, (me + offset) % size, 0, keepdims=False)

    far = block(2)
    up = lax.ppermute(
        jnp.concatenate([block(1), far[:cut]], 0), axis_name, shift_pairs(size, 1)
    )
    down = lax.ppermute(
        jnp.concatenate([block(-1), far[cut:]], 0), axis_name, shift_pairs(size, -1)
    )
    far_top = lax.ppermute(up[rows:], axis_name, shift_pairs(size, 1))
    far_bottom = lax.ppermute(down[rows:], axis_name, shift_pairs(size, -1))
    got = block(0).astype(jnp.float32) + up[:rows].astype(jnp.float32)
    got = got + down[:rows].astype(jnp.float32)
    return got + jnp.concatenate([far_top, far_bottom], 0).astype(jnp.float32)


def modulate_blocks(blocks, mods, width):
    values = [b.astype(jnp.float32) for b in blocks]
    mean = sum(jnp.sum(v, -1, keepdims=True) for v in values) / width
    centred = [v - mean for v in values]
    spread = sum(jnp.sum(c * c, -1, keepdims=True) for c in centred) / width
    scale = lax.rsqrt(spread + 1e-06)
    out = []
    for c, m in zip(centred, mods):
        m = m.astype(jnp.float32)
        out.append(((c * scale) * (1.0 + m[1:2]) + m[0:1]).astype(jnp.bfloat16))
    return jnp.concatenate(out, -1)


def order_blocks(by_offset, me, size):
    stacked = jnp.stack(by_offset)
    return [
        lax.dynamic_index_in_dim(stacked, (k - me) % size, 0, keepdims=False) for k in range(size)
    ]


def add_rows(piece, ready):
    return jnp.einsum("ti,sin->tsn", ready, piece, preferred_element_type=jnp.float32)


def layer(
    img_tokens,
    txt_tokens,
    img_mod,
    txt_mod,
    img_gate,
    txt_len,
    img_qkv_weight,
    txt_kv_weight,
    out_weight,
    final_weight,
    latent,
    sigmas,
    step_index,
    guidance,
):
    n_row = 4
    images = img_tokens.shape[2]
    text_slots = txt_tokens.shape[2]
    local_width = img_qkv_weight.shape[2]
    width = local_width * n_row
    me_row = lax.axis_index("row")
    core = lax.axis_index("cfg")

    img_blocks = order_blocks(ring_gather(img_tokens[0, 0], "row", n_row), me_row, n_row)
    txt_bundle = jnp.concatenate([txt_tokens[0, 0], img_mod[0, 0], txt_mod[0, 0]], 0)
    txt_blocks = order_blocks(ring_gather(txt_bundle, "row", n_row), me_row, n_row)
    img_ready = modulate_blocks(
        img_blocks, [b[text_slots : text_slots + 2] for b in txt_blocks], width
    )
    txt_ready = modulate_blocks(
        [b[:text_slots] for b in txt_blocks],
        [b[text_slots + 2 : text_slots + 4] for b in txt_blocks],
        width,
    )
    half = local_width // 2
    swap = [(0, 1), (1, 0)]

    def own_half(weight, axis):
        return lax.dynamic_slice_in_dim(weight, core * half, half, axis=axis)

    img_piece = jnp.transpose(own_half(img_qkv_weight, 2), (1, 0, 2))
    img_w = lax.all_gather(img_piece, "col", axis=1, tiled=True)
    txt_out_piece = jnp.concatenate(
        [jnp.transpose(own_half(txt_kv_weight, 2), (1, 0, 2)), own_half(out_weight, 0).T[None]], 0
    )
    img_w, txt_out_piece = lax.optimization_barrier((img_w, txt_out_piece))
    txt_out_w = lax.all_gather(txt_out_piece, "col", axis=1, tiled=True)
    txt_w = txt_out_w[:2]
    out_w = txt_out_w[2]
    img_w_other = lax.ppermute(img_w, "cfg", swap)
    halves = [
        (txt_w, img_w, out_w),
        (lax.ppermute(txt_w, "cfg", swap), img_w_other, lax.ppermute(out_w, "cfg", swap)),
    ]
    positions = jnp.arange(text_slots + images, dtype=jnp.int32)
    usable = (positions < txt_len[0, 0]) | (positions >= text_slots)
    heads_half = half // HD

    def project(txt_w, img_w):
        img_proj = add_rows(img_w, img_ready).reshape(images, 3, heads_half, HD)
        txt_proj = add_rows(txt_w, txt_ready).reshape(text_slots, 2, heads_half, HD)
        queries = rms_norm(img_proj[:, 0]).astype(jnp.bfloat16)
        key_rows = jnp.concatenate(
            [rms_norm(txt_proj[:, 0]), rms_norm(img_proj[:, 1])], 0
        ).astype(jnp.bfloat16)
        value_rows = jnp.concatenate([txt_proj[:, 1], img_proj[:, 2]], 0).astype(jnp.bfloat16)
        return queries, key_rows, value_rows

    def attend(queries, key_rows, value_rows, out_w):
        scores = jnp.einsum(
            "qhe,khe->hqk", queries, key_rows, preferred_element_type=jnp.float32
        ) / math.sqrt(HD)
        weights = jnp.where(usable, jnp.exp(scores), 0.0)
        chances = (weights / jnp.sum(weights, -1, keepdims=True)).astype(jnp.bfloat16)
        mixed = jnp.einsum("hqk,khe->qhe", chances, value_rows, preferred_element_type=jnp.float32)
        outputs = mixed.reshape(queries.shape[0], half).astype(jnp.bfloat16)
        return jnp.einsum(
            "ti,koi->kto",
            outputs,
            out_w.reshape(n_row, local_width, half),
            preferred_element_type=jnp.float32,
        )

    projections = [project(*h[:2]) for h in halves]
    n_chunk = 4
    chunk = images // n_chunk
    pieces = []
    for c in range(n_chunk):
        part = 0.0
        for (queries, key_rows, value_rows), h in zip(projections, halves):
            part = part + attend(queries[c * chunk : (c + 1) * chunk], key_rows, value_rows, h[2])
        term_blocks = part.astype(jnp.bfloat16)
        got = reduce_blocks(term_blocks, me_row, "row", n_row)
        pieces.append(got)
    projected = jnp.concatenate(pieces, 0)
    gating = img_gate[0].astype(jnp.float32)
    img_out = (img_tokens[0, 0].astype(jnp.float32) + gating * projected).astype(jnp.bfloat16)
    velocity = jnp.dot(img_out, final_weight, preferred_element_type=jnp.float32)
    strength = guidance[0]
    share = jnp.where(core == 1, strength, 1.0 - strength)
    weighted = velocity * share
    n_pair = 2 * n_row
    me_pair = core * n_row + me_row
    rows_each = weighted.shape[0] // n_pair
    velocity_blocks = weighted.reshape(n_pair, rows_each, weighted.shape[1])
    guided = lax.dynamic_index_in_dim(velocity_blocks, me_pair, 0, keepdims=False)
    for step in range(1, n_pair):
        outgoing = lax.dynamic_index_in_dim(velocity_blocks, (me_pair + step) % n_pair, 0, keepdims=False)
        guided = guided + lax.ppermute(outgoing, ("cfg", "row"), shift_pairs(n_pair, step))
    position_now = step_index[0]
    step_size = sigmas[position_now + 1] - sigmas[position_now]
    return (img_out[None, None], latent + step_size * guided[None])


def solution(mesh):
    return jax.shard_map(
        layer,
        mesh=mesh,
        in_specs=(
            P("cfg", "col", None, "row"),
            P("cfg", "col", None, "row"),
            P("cfg", "col", None, "row"),
            P("cfg", "col", None, "row"),
            P("cfg", "col", "row"),
            P("cfg", "col"),
            P("col", None, "row"),
            P("col", None, "row"),
            P("row", "col"),
            P("row", None),
            P("col", ("cfg", "row"), None),
            P(),
            P(),
            P(),
        ),
        out_specs=(P("cfg", "col", None, "row"), P("col", ("cfg", "row"), None)),
        check_vma=False,
    )
```

```python
import math

import jax
import jax.numpy as jnp
from jax import lax
from jax.sharding import PartitionSpec as P


HD = 128


def rms_norm(values):
    return values * lax.rsqrt(jnp.mean(values * values, -1, keepdims=True) + 1e-06)


def shift_pairs(size, step):
    return [(i, (i + step) % size) for i in range(size)]


def ring_gather(piece, axis_name, size):
    assert size == 4
    from_prev = lax.ppermute(piece, axis_name, shift_pairs(size, 1))
    from_next = lax.ppermute(piece, axis_name, shift_pairs(size, -1))
    cut = piece.shape[0] // 2
    far_top = lax.ppermute(from_prev[:cut], axis_name, shift_pairs(size, 1))
    far_bottom = lax.ppermute(from_next[cut:], axis_name, shift_pairs(size, -1))
    far = jnp.concatenate([far_top, far_bottom], 0)
    return [piece, from_next, far, from_prev]


def reduce_blocks(term_blocks, me, axis_name, size):
    assert size == 4
    rows = term_blocks.shape[1]
    cut = rows // 2

    def block(offset):
        return lax.dynamic_index_in_dim(term_blocks, (me + offset) % size, 0, keepdims=False)

    far = block(2)
    up = lax.ppermute(jnp.concatenate([block(1), far[:cut]], 0), axis_name, shift_pairs(size, 1))
    down = lax.ppermute(
        jnp.concatenate([block(-1), far[cut:]], 0), axis_name, shift_pairs(size, -1)
    )
    far_top = lax.ppermute(up[rows:], axis_name, shift_pairs(size, 1))
    far_bottom = lax.ppermute(down[rows:], axis_name, shift_pairs(size, -1))
    got = block(0).astype(jnp.float32) + up[:rows].astype(jnp.float32)
    got = got + down[:rows].astype(jnp.float32)
    return got + jnp.concatenate([far_top, far_bottom], 0).astype(jnp.float32)


def modulate_blocks(blocks, mods, width):
    values = [b.astype(jnp.float32) for b in blocks]
    mean = sum(jnp.sum(v, -1, keepdims=True) for v in values) / width
    centred = [v - mean for v in values]
    spread = sum(jnp.sum(c * c, -1, keepdims=True) for c in centred) / width
    scale = lax.rsqrt(spread + 1e-06)
    out = []
    for c, m in zip(centred, mods):
        m = m.astype(jnp.float32)
        out.append(((c * scale) * (1.0 + m[1:2]) + m[0:1]).astype(jnp.bfloat16))
    return jnp.concatenate(out, -1)


def order_blocks(by_offset, me, size):
    stacked = jnp.stack(by_offset)
    return [
        lax.dynamic_index_in_dim(stacked, (k - me) % size, 0, keepdims=False) for k in range(size)
    ]


def add_rows(piece, ready):
    return jnp.einsum("ti,sin->tsn", ready, piece, preferred_element_type=jnp.float32)


def layer(
    img_tokens,
    txt_tokens,
    img_mod,
    txt_mod,
    img_gate,
    txt_len,
    img_qkv_weight,
    txt_kv_weight,
    out_weight,
    final_weight,
    latent,
    sigmas,
    step_index,
    guidance,
):
    n_row = 4
    images = img_tokens.shape[2]
    text_slots = txt_tokens.shape[2]
    local_width = img_qkv_weight.shape[2]
    width = local_width * n_row
    me_row = lax.axis_index("row")
    core = lax.axis_index("cfg")

    img_blocks = order_blocks(ring_gather(img_tokens[0, 0], "row", n_row), me_row, n_row)
    txt_bundle = jnp.concatenate([txt_tokens[0, 0], img_mod[0, 0], txt_mod[0, 0]], 0)
    txt_blocks = order_blocks(ring_gather(txt_bundle, "row", n_row), me_row, n_row)
    img_ready = modulate_blocks(
        img_blocks, [b[text_slots : text_slots + 2] for b in txt_blocks], width
    )
    txt_ready = modulate_blocks(
        [b[:text_slots] for b in txt_blocks],
        [b[text_slots + 2 : text_slots + 4] for b in txt_blocks],
        width,
    )
    half = local_width // 2
    swap = [(0, 1), (1, 0)]

    def own_half(weight, axis):
        return lax.dynamic_slice_in_dim(weight, core * half, half, axis=axis)

    img_piece = jnp.transpose(own_half(img_qkv_weight, 2), (1, 0, 2))
    img_w = lax.all_gather(img_piece, "col", axis=1, tiled=True)
    txt_out_piece = jnp.concatenate(
        [jnp.transpose(own_half(txt_kv_weight, 2), (1, 0, 2)), own_half(out_weight, 0).T[None]], 0
    )
    img_w, txt_out_piece = lax.optimization_barrier((img_w, txt_out_piece))
    txt_out_w = lax.all_gather(txt_out_piece, "col", axis=1, tiled=True)
    txt_w = txt_out_w[:2]
    out_w = txt_out_w[2]
    img_w_other = lax.ppermute(img_w, "cfg", swap)
    halves = [
        (txt_w, img_w, out_w),
        (lax.ppermute(txt_w, "cfg", swap), img_w_other, lax.ppermute(out_w, "cfg", swap)),
    ]
    positions = jnp.arange(text_slots + images, dtype=jnp.int32)
    usable = (positions < txt_len[0, 0]) | (positions >= text_slots)
    heads_half = half // HD

    def project(txt_w, img_w):
        img_proj = add_rows(img_w, img_ready).reshape(images, 3, heads_half, HD)
        txt_proj = add_rows(txt_w, txt_ready).reshape(text_slots, 2, heads_half, HD)
        queries = rms_norm(img_proj[:, 0]).astype(jnp.bfloat16)
        key_rows = jnp.concatenate(
            [rms_norm(txt_proj[:, 0]), rms_norm(img_proj[:, 1])], 0
        ).astype(jnp.bfloat16)
        value_rows = jnp.concatenate([txt_proj[:, 1], img_proj[:, 2]], 0).astype(jnp.bfloat16)
        return queries, key_rows, value_rows

    def attend(queries, key_rows, value_rows, out_w):
        scores = jnp.einsum(
            "qhe,khe->hqk", queries, key_rows, preferred_element_type=jnp.float32
        ) / math.sqrt(HD)
        weights = jnp.where(usable, jnp.exp(scores), 0.0)
        chances = (weights / jnp.sum(weights, -1, keepdims=True)).astype(jnp.bfloat16)
        mixed = jnp.einsum("hqk,khe->qhe", chances, value_rows, preferred_element_type=jnp.float32)
        outputs = mixed.reshape(queries.shape[0], half).astype(jnp.bfloat16)
        return jnp.einsum(
            "ti,koi->kto",
            outputs,
            out_w.reshape(n_row, local_width, half),
            preferred_element_type=jnp.float32,
        )

    projections = [project(*h[:2]) for h in halves]
    n_chunk = 2
    chunk = images // n_chunk
    pieces = []
    for c in range(n_chunk):
        part = 0.0
        for (queries, key_rows, value_rows), h in zip(projections, halves):
            part = part + attend(queries[c * chunk : (c + 1) * chunk], key_rows, value_rows, h[2])
        term_blocks = part.astype(jnp.bfloat16)
        got = reduce_blocks(term_blocks, me_row, "row", n_row)
        pieces.append(got)
    projected = jnp.concatenate(pieces, 0)
    gating = img_gate[0].astype(jnp.float32)
    img_out = (img_tokens[0, 0].astype(jnp.float32) + gating * projected).astype(jnp.bfloat16)
    velocity = jnp.dot(img_out, final_weight, preferred_element_type=jnp.float32)
    strength = guidance[0]
    share = jnp.where(core == 1, strength, 1.0 - strength)
    weighted = velocity * share
    both = weighted + lax.ppermute(weighted, "cfg", [(0, 1), (1, 0)])
    n_pair = 2 * n_row
    rows_each = both.shape[0] // n_pair
    velocity_blocks = both.reshape(n_pair, rows_each, both.shape[1])
    guided = lax.dynamic_index_in_dim(velocity_blocks, core * n_row + me_row, 0, keepdims=False)
    for step in range(1, n_row):
        outgoing = lax.dynamic_index_in_dim(
            velocity_blocks, core * n_row + (me_row + step) % n_row, 0, keepdims=False
        )
        guided = guided + lax.ppermute(outgoing, "row", shift_pairs(n_row, step))
    position_now = step_index[0]
    step_size = sigmas[position_now + 1] - sigmas[position_now]
    return (img_out[None, None], latent + step_size * guided[None])


def solution(mesh):
    return jax.shard_map(
        layer,
        mesh=mesh,
        in_specs=(
            P("cfg", "col", None, "row"),
            P("cfg", "col", None, "row"),
            P("cfg", "col", None, "row"),
            P("cfg", "col", None, "row"),
            P("cfg", "col", "row"),
            P("cfg", "col"),
            P("col", None, "row"),
            P("col", None, "row"),
            P("row", "col"),
            P("row", None),
            P("col", ("cfg", "row"), None),
            P(),
            P(),
            P(),
        ),
        out_specs=(P("cfg", "col", None, "row"), P("col", ("cfg", "row"), None)),
        check_vma=False,
    )
```
